256 devices in a mesh: dp: 16 (over z_lo, x, core), fsdp: 16 (over y, z_hi).
Axes of the slice: x: 4, y: 4, z: 8 (z_hi: 4, z_lo: 2; z = z_hi * 2 + z_lo), core: 2. Of those that a mesh axis runs over, the one named last changes fastest.
Arguments:
- hidden_in: bfloat16 [131072, 1536], P(('dp', 'fsdp')), may hold values from -6 to 6
- grad_out: bfloat16 [131072, 1536], P(('dp', 'fsdp')), may hold values from -6 to 6
- lengths: int32 [256, 3], P(('dp', 'fsdp')), may hold values from 1 to 510, as said below
- conv_kernel: float32 [5, 1536], replicated, may hold values from -3 to 3
- norm_gain: float32 [1536], replicated, may hold values from 0.5 to 2
- out_weight: bfloat16 [1536, 1536], P('fsdp'), may hold values from -0.15625 to 0.15625
Outputs:
- output: float32 [131072, 1536], P(('dp', 'fsdp'))
- grad_hidden: float32 [131072, 1536], P(('dp', 'fsdp'))
- grad_weight: float32 [1536, 1536], P('fsdp')
- grad_kernel: float32 [5, 1536], replicated
- grad_gain: float32 [1536], replicated
The draws below stay inside these ranges and needn't reach their ends.
Inputs may be any that keep to these rules, and one draw needn't show every extreme that they name: `lengths`: each row sums to at most 512. A row whose sum exceeds (3) * 128 sums to exactly 512, holds 2 utterances of length 1 followed by one of length 510, and then the row with the same fsdp index whose dp index differs by half the dp axis sums to at most (2) * 128; every other row sums to at most (3) * 128. Some row in every draw sums to 512.
All inputs are finite; a program needn't handle non-finite values.
Results may differ from the reference program's by a relative error of at most 0.003.
Values may be sent and summed in bfloat16 or wider, within the bound.
No kernel may reach another device: no remote copies, remote signals or barrier semaphores. Data moves between devices by JAX's collectives and lax.ppermute only.
A program may use at most 128 MiB of HBM per device.

```python
import math
import jax
import jax.numpy as jnp
from jax import lax

C = 1536
D = 1536
KSIZE = 5
BLOCK = 128
UTTS = 3
NB = 4
FRAMES = 131072
N_DP = 16
N_FSDP = 16


def draw_lengths(key, part):
    count = N_DP * N_FSDP
    half = N_DP // 2
    pairs = half * N_FSDP
    keys = jax.random.split(jax.random.fold_in(key, 11), 4)
    state = jax.random.randint(keys[0], (pairs,), 0, 3)
    forced = jax.random.randint(keys[1], (), 0, pairs)
    state = jnp.where(jnp.arange(pairs) == forced, 1 + state % 2, state)
    device = jnp.arange(count, dtype=jnp.int32)
    dp_index = device // N_FSDP
    fsdp_index = device % N_FSDP
    lower = dp_index < half
    pair_index = dp_index % half * N_FSDP + fsdp_index
    chosen = state[pair_index]
    heavy = (chosen == 1) & lower | (chosen == 2) & ~lower
    light = (chosen == 1) & ~lower | (chosen == 2) & lower
    full = NB * BLOCK
    upper = jnp.where(light, (NB - 2) * BLOCK, (NB - 1) * BLOCK)
    spread = jax.random.randint(keys[2], (count,), 0, 1 << 20)
    total = jnp.where(heavy, full, UTTS + spread % (upper - UTTS + 1))
    share = total // UTTS
    raw = jax.random.randint(keys[3], (count, UTTS), 0, 1 << 20)
    first = 1 + raw[:, :UTTS - 1] % share[:, None]
    first = jnp.where(heavy[:, None], 1, first)
    last = total - jnp.sum(first, axis=1)
    return jnp.concatenate([first, last[:, None]], axis=1).astype(jnp.int32)


def block_levels(key, extent, cuts, smallest, largest):
    def one(axis_at, blocks):
        heights = jax.random.uniform(jax.random.fold_in(jax.random.fold_in(key, 6), axis_at), (blocks,), jnp.float32, smallest / len(cuts), largest / len(cuts))
        return jnp.repeat(jnp.exp(heights), extent[axis_at] // blocks).reshape((-1,) + (1,) * (len(extent) - axis_at - 1))

    factor_of = one(*cuts[0])
    for cut in cuts[1:]:
        factor_of = factor_of * one(*cut)
    return factor_of


def gaussian(key, extent, width, most, cuts=(), kind=jnp.bfloat16):
    values = width * jax.random.normal(key, extent, jnp.float32)
    if cuts:
        values = values * block_levels(key, extent, cuts, -0.22, 0.18)
    return jnp.clip(values, -most, most).astype(kind)


def setup_inputs(seed: int = 0) -> dict:
    splits = jax.random.split(jax.random.key(seed), 7)
    hidden_in = gaussian(splits[0], (FRAMES, C), 1.0, 6.0, ((0, 256),))
    grad_out = gaussian(splits[1], (FRAMES, D), 1.0, 6.0, ((0, 256),))
    lengths = draw_lengths(jax.random.fold_in(splits[6], 71), 0)
    conv_kernel = gaussian(splits[3], (KSIZE, C), 0.5, 3.0, (), jnp.float32)
    norm_gain = jnp.clip(jnp.exp(jax.random.uniform(splits[4], (C,), jnp.float32, math.log(0.5), math.log(2.0))), 0.5, 2.0)
    out_weight = gaussian(splits[5], (C, D), C ** -0.5, 0.15625, ((0, 16),))
    return {"hidden_in": hidden_in, "grad_out": grad_out, "lengths": lengths, "conv_kernel": conv_kernel, "norm_gain": norm_gain, "out_weight": out_weight}


def tap_mask(lengths, frames, count):
    utt_ends = jnp.cumsum(lengths)
    position = jnp.arange(frames, dtype=jnp.int32)
    segment_id = lax.optimization_barrier(jnp.sum((position[:, None] >= utt_ends[None, :]).astype(jnp.int32), axis=1))
    inside = position < utt_ends[-1]
    half_width = count // 2
    segment_pad = jnp.pad(segment_id, half_width, constant_values=-1)
    inside_pad = jnp.pad(inside, half_width, constant_values=False)
    rows_out = []
    for k in range(count):
        same = (segment_pad[k:k + frames] == segment_id) & inside_pad[k:k + frames] & inside
        rows_out.append(same.astype(jnp.float32))
    return jnp.stack(rows_out)

def conv_front(extended, taps, conv_kernel, norm_gain):
    length = taps.shape[2]
    mixed = jnp.zeros((taps.shape[0], length, extended.shape[2]), jnp.float32)
    for k in range(conv_kernel.shape[0]):
        mixed = mixed + conv_kernel[k] * extended[:, k:k + length].astype(jnp.float32) * taps[:, k, :, None]
    centred = mixed - lax.optimization_barrier(jnp.mean(mixed, axis=-1, keepdims=True))
    inverse = lax.rsqrt(lax.optimization_barrier(jnp.mean(centred * centred, axis=-1, keepdims=True)) + 1e-05)
    normed = centred * inverse
    scaled = normed * norm_gain
    squash = jax.nn.sigmoid(scaled)
    live_rows = taps[:, conv_kernel.shape[0] // 2, :, None]
    activation = (scaled * squash * live_rows).astype(jnp.bfloat16)
    return (activation, normed, inverse, scaled, squash, live_rows)

def conv_back(extended, taps, conv_kernel, norm_gain, grad_act, normed, inverse, scaled, squash, live_rows):
    length = taps.shape[2]
    grad_scaled = grad_act * live_rows * squash * (1.0 + scaled * (1.0 - squash))
    gain_grad = lax.optimization_barrier(jnp.sum(grad_scaled * normed, axis=(0, 1)))
    grad_normed = grad_scaled * norm_gain
    grad_pre = inverse * (grad_normed - lax.optimization_barrier(jnp.mean(grad_normed, axis=-1, keepdims=True)) - normed * lax.optimization_barrier(jnp.mean(grad_normed * normed, axis=-1, keepdims=True)))
    grad_ext = jnp.zeros(extended.shape, jnp.float32)
    kernel_rows = []
    for k in range(conv_kernel.shape[0]):
        weighted = grad_pre * taps[:, k, :, None]
        kernel_rows.append(lax.optimization_barrier(jnp.sum(weighted * extended[:, k:k + length].astype(jnp.float32), axis=(0, 1))))
        grad_ext = grad_ext.at[:, k:k + length].add(conv_kernel[k] * weighted)
    return (grad_ext, jnp.stack(kernel_rows), gain_grad)

def reference(hidden_in, grad_out, lengths, conv_kernel, norm_gain, out_weight):
    frames = NB * BLOCK
    count = conv_kernel.shape[0]
    half_width = count // 2
    device_rows = lengths.shape[0]
    hidden_dev = hidden_in.reshape(device_rows, frames, C)
    cot_dev = grad_out.reshape(device_rows, frames, D)

    def one_device(carry, item):
        hidden_part, cot_part, lens = item
        taps = tap_mask(lens, frames, count)[None]
        extended = jnp.pad(hidden_part, ((half_width, half_width), (0, 0)))[None]
        activation, normed, inverse, scaled, squash, live_rows = conv_front(extended, taps, conv_kernel, norm_gain)
        flat_act = activation[0]
        produced = jnp.dot(flat_act, out_weight, preferred_element_type=jnp.float32)
        grad_act = lax.dot_general(cot_part, out_weight, (((1,), (1,)), ((), ())), preferred_element_type=jnp.float32)
        grad_ext, kernel_grad, gain_grad = conv_back(extended, taps, conv_kernel, norm_gain, grad_act[None], normed, inverse, scaled, squash, live_rows)
        grad_rows = grad_ext[0, half_width:half_width + frames]
        weight_term = lax.dot_general(flat_act, cot_part, (((0,), (0,)), ((), ())), preferred_element_type=jnp.float32)
        return ((carry[0] + weight_term, carry[1] + kernel_grad, carry[2] + gain_grad), (produced, grad_rows))
    start = (jnp.zeros((C, D), jnp.float32), jnp.zeros((count, C), jnp.float32), jnp.zeros((C,), jnp.float32))
    sums, outs_dev = lax.scan(one_device, start, (hidden_dev, cot_dev, lengths))
    factor = 1.0 / math.sqrt(FRAMES)
    return (outs_dev[0].reshape(-1, D), outs_dev[1].reshape(-1, C), sums[0] * factor, sums[1] * factor, sums[2] * factor)
```

```python
import math

import jax
import jax.numpy as jnp
from jax import lax
from jax.sharding import PartitionSpec as P


def tap_mask(lengths, frames, count):
    utt_ends = jnp.cumsum(lengths)
    position = jnp.arange(frames, dtype=jnp.int32)
    segment_id = jnp.sum((position[:, None] >= utt_ends[None, :]).astype(jnp.int32), axis=1)
    inside = position < utt_ends[-1]
    half_width = count // 2
    segment_pad = jnp.pad(segment_id, half_width, constant_values=-1)
    inside_pad = jnp.pad(inside, half_width, constant_values=False)
    rows_out = []
    for k in range(count):
        same = (segment_pad[k : k + frames] == segment_id) & inside_pad[k : k + frames] & inside
        rows_out.append(same.astype(jnp.float32))
    return jnp.stack(rows_out)


def shifted(x, half_width):
    frames = x.shape[0]
    padded = jnp.pad(x, ((half_width, half_width), (0, 0)))
    return [padded[k : k + frames] for k in range(2 * half_width + 1)]


def butterfly(x, axis):
    size = lax.axis_size(axis)
    step = 1
    while step < size:
        pairs = [(i, i ^ step) for i in range(size)]
        x = x + lax.ppermute(x, axis, pairs)
        step *= 2
    return x


def shards(hidden_in, grad_out, lengths, conv_kernel, norm_gain, out_weight):
    frames, chans = hidden_in.shape
    count = conv_kernel.shape[0]
    half_width = count // 2
    full_weight = lax.all_gather(out_weight, "fsdp", axis=0, tiled=True)
    taps = tap_mask(lengths[0], frames, count)
    live = taps[half_width][:, None]
    views = shifted(hidden_in, half_width)
    mixed = jnp.zeros((frames, chans), jnp.float32)
    for k in range(count):
        mixed = mixed + conv_kernel[k] * views[k].astype(jnp.float32) * taps[k][:, None]
    centred = mixed - jnp.mean(mixed, axis=-1, keepdims=True)
    inverse = lax.rsqrt(jnp.mean(centred * centred, axis=-1, keepdims=True) + 1e-05)
    normed = centred * inverse
    scaled = normed * norm_gain
    squash = jax.nn.sigmoid(scaled)
    activation = (scaled * squash * live).astype(jnp.bfloat16)
    weight_terms = lax.dot_general(
        activation, grad_out, (((0,), (0,)), ((), ())), preferred_element_type=jnp.float32
    )
    shard_sum = lax.psum_scatter(weight_terms, "fsdp", scatter_dimension=0, tiled=True)
    output = jnp.dot(activation, full_weight, preferred_element_type=jnp.float32)
    grad_act = lax.dot_general(
        grad_out, full_weight, (((1,), (1,)), ((), ())), preferred_element_type=jnp.float32
    )
    grad_scaled = grad_act * live * squash * (1.0 + scaled * (1.0 - squash))
    gain_grad = jnp.sum(grad_scaled * normed, axis=0)
    grad_normed = grad_scaled * norm_gain
    grad_mixed = inverse * (
        grad_normed
        - jnp.mean(grad_normed, axis=-1, keepdims=True)
        - normed * jnp.mean(grad_normed * normed, axis=-1, keepdims=True)
    )
    kernel_rows = []
    for k in range(count):
        weighted = grad_mixed * taps[k][:, None]
        kernel_rows.append(jnp.sum(weighted * views[k].astype(jnp.float32), axis=0))
    back_views = shifted(grad_mixed, half_width)
    grad_hidden = jnp.zeros((frames, chans), jnp.float32)
    for k in range(count):
        grad_hidden = grad_hidden + conv_kernel[k] * (
            back_views[count - 1 - k] * taps[count - 1 - k][:, None]
        )
    small = jnp.concatenate([jnp.stack(kernel_rows), gain_grad[None]], axis=0)
    small = butterfly(small, "fsdp")
    total = butterfly(jnp.concatenate([shard_sum, small], axis=0), "dp")
    rows = shard_sum.shape[0]
    dp_count = lax.axis_size("dp")
    fsdp_count = lax.axis_size("fsdp")
    factor = 1.0 / math.sqrt(frames * dp_count * fsdp_count)
    weight_sum = total[:rows] * factor
    kernel_sum = total[rows : rows + count] * factor
    gain_sum = total[rows + count] * factor
    return (output, grad_hidden, weight_sum, kernel_sum, gain_sum)


def solution(mesh):
    placed = (
        P(("dp", "fsdp"), None),
        P(("dp", "fsdp"), None),
        P(("dp", "fsdp"), None),
        P(),
        P(),
        P("fsdp", None),
    )
    return jax.shard_map(
        shards,
        mesh=mesh,
        in_specs=placed,
        out_specs=(P(("dp", "fsdp"), None), P(("dp", "fsdp"), None), P("fsdp", None), P(), P()),
        check_vma=False,
    )
```

```python
import math

import jax
import jax.numpy as jnp
from jax import lax
from jax.sharding import PartitionSpec as P


def tap_mask(lengths, frames, count):
    utt_ends = jnp.cumsum(lengths)
    position = jnp.arange(frames, dtype=jnp.int32)
    segment_id = jnp.sum((position[:, None] >= utt_ends[None, :]).astype(jnp.int32), axis=1)
    inside = position < utt_ends[-1]
    half_width = count // 2
    segment_pad = jnp.pad(segment_id, half_width, constant_values=-1)
    inside_pad = jnp.pad(inside, half_width, constant_values=False)
    rows_out = []
    for k in range(count):
        same = (segment_pad[k : k + frames] == segment_id) & inside_pad[k : k + frames] & inside
        rows_out.append(same.astype(jnp.float32))
    return jnp.stack(rows_out)


def shifted(x, half_width):
    frames = x.shape[0]
    padded = jnp.pad(x, ((half_width, half_width), (0, 0)))
    return [padded[k : k + frames] for k in range(2 * half_width + 1)]


def butterfly(x, axis, steps):
    size = lax.axis_size(axis)
    for step in steps:
        pairs = [(i, i ^ step) for i in range(size)]
        x = x + lax.ppermute(x, axis, pairs)
    return x


def sibling(x):
    size = lax.axis_size("dp")
    return lax.ppermute(x, "dp", [(i, i ^ 1) for i in range(size)])


def shards(hidden_in, grad_out, lengths, conv_kernel, norm_gain, out_weight):
    frames, chans = hidden_in.shape
    width = grad_out.shape[1]
    count = conv_kernel.shape[0]
    half_width = count // 2
    fsdp_count = lax.axis_size("fsdp")
    dp_count = lax.axis_size("dp")
    rows = out_weight.shape[0]
    half_rows = rows // 2
    core = lax.axis_index("dp") % 2
    gathered = lax.all_gather(out_weight, "fsdp", axis=0, tiled=True)
    taps = tap_mask(lengths[0], frames, count)
    live = taps[half_width][:, None]
    views = shifted(hidden_in, half_width)
    mixed = jnp.zeros((frames, chans), jnp.float32)
    for k in range(count):
        mixed = mixed + conv_kernel[k] * views[k].astype(jnp.float32) * taps[k][:, None]
    centred = mixed - jnp.mean(mixed, axis=-1, keepdims=True)
    inverse = lax.rsqrt(jnp.mean(centred * centred, axis=-1, keepdims=True) + 1e-05)
    normed = centred * inverse
    scaled = normed * norm_gain
    squash = jax.nn.sigmoid(scaled)
    activation = (scaled * squash * live).astype(jnp.bfloat16)
    split_act = activation.reshape(frames, fsdp_count, 2, half_rows)
    keep_act = lax.dynamic_index_in_dim(split_act, core, 2, keepdims=False).reshape(frames, -1)
    send_act = lax.dynamic_index_in_dim(split_act, 1 - core, 2, keepdims=False).reshape(frames, -1)
    contract = (((0,), (0,)), ((), ()))
    keep_terms = lax.dot_general(keep_act, grad_out, contract, preferred_element_type=jnp.float32)
    send_terms = lax.dot_general(send_act, grad_out, contract, preferred_element_type=jnp.float32)
    chip_terms = keep_terms + sibling(send_terms)
    gathered, chip_terms, activation = lax.optimization_barrier((gathered, chip_terms, activation))
    shard_sum = lax.psum_scatter(chip_terms, "fsdp", scatter_dimension=0, tiled=True)
    full_weight = gathered
    output = jnp.dot(activation, full_weight, preferred_element_type=jnp.float32)
    grad_act = lax.dot_general(
        grad_out, full_weight, (((1,), (1,)), ((), ())), preferred_element_type=jnp.float32
    )
    grad_scaled = grad_act * live * squash * (1.0 + scaled * (1.0 - squash))
    gain_grad = jnp.sum(grad_scaled * normed, axis=0)
    grad_normed = grad_scaled * norm_gain
    grad_mixed = inverse * (
        grad_normed
        - jnp.mean(grad_normed, axis=-1, keepdims=True)
        - normed * jnp.mean(grad_normed * normed, axis=-1, keepdims=True)
    )
    kernel_rows = []
    for k in range(count):
        weighted = grad_mixed * taps[k][:, None]
        kernel_rows.append(jnp.sum(weighted * views[k].astype(jnp.float32), axis=0))
    back_views = shifted(grad_mixed, half_width)
    grad_hidden = jnp.zeros((frames, chans), jnp.float32)
    for k in range(count):
        grad_hidden = grad_hidden + conv_kernel[k] * (
            back_views[count - 1 - k] * taps[count - 1 - k][:, None]
        )
    small = jnp.concatenate([jnp.stack(kernel_rows), gain_grad[None]], axis=0)
    small = butterfly(small, "fsdp", (1, 2, 4, 8))
    small = butterfly(small, "dp", (1, 2, 4, 8))
    shard_sum, small = lax.optimization_barrier((shard_sum, small))
    half_sum = butterfly(shard_sum, "dp", (2, 4, 8))
    other_sum = sibling(half_sum)
    weight_sum = jnp.where(
        core == 0,
        jnp.concatenate([half_sum, other_sum], axis=0),
        jnp.concatenate([other_sum, half_sum], axis=0),
    )
    factor = 1.0 / math.sqrt(frames * dp_count * fsdp_count)
    return (
        output,
        grad_hidden,
        weight_sum * factor,
        small[:count] * factor,
        small[count] * factor,
    )


def solution(mesh):
    placed = (
        P(("dp", "fsdp"), None),
        P(("dp", "fsdp"), None),
        P(("dp", "fsdp"), None),
        P(),
        P(),
        P("fsdp", None),
    )
    return jax.shard_map(
        shards,
        mesh=mesh,
        in_specs=placed,
        out_specs=(P(("dp", "fsdp"), None), P(("dp", "fsdp"), None), P("fsdp", None), P(), P()),
        check_vma=False,
    )
```

```python
import math

import jax
import jax.numpy as jnp
from jax import lax
from jax.sharding import PartitionSpec as P


def tap_mask(lengths, frames, count):
    utt_ends = jnp.cumsum(lengths)
    position = jnp.arange(frames, dtype=jnp.int32)
    segment_id = jnp.sum((position[:, None] >= utt_ends[None, :]).astype(jnp.int32), axis=1)
    inside = position < utt_ends[-1]
    half_width = count // 2
    segment_pad = jnp.pad(segment_id, half_width, constant_values=-1)
    inside_pad = jnp.pad(inside, half_width, constant_values=False)
    rows_out = []
    for k in range(count):
        same = (segment_pad[k : k + frames] == segment_id) & inside_pad[k : k + frames] & inside
        rows_out.append(same.astype(jnp.float32))
    return jnp.stack(rows_out)


def shifted(x, half_width):
    frames = x.shape[0]
    padded = jnp.pad(x, ((half_width, half_width), (0, 0)))
    return [padded[k : k + frames] for k in range(2 * half_width + 1)]


def butterfly(x, axis, steps):
    size = lax.axis_size(axis)
    for step in steps:
        pairs = [(i, i ^ step) for i in range(size)]
        x = x + lax.ppermute(x, axis, pairs)
    return x


def sibling(x):
    size = lax.axis_size("dp")
    return lax.ppermute(x, "dp", [(i, i ^ 1) for i in range(size)])


def shards(hidden_in, grad_out, lengths, conv_kernel, norm_gain, out_weight):
    frames, chans = hidden_in.shape
    width = grad_out.shape[1]
    count = conv_kernel.shape[0]
    half_width = count // 2
    fsdp_count = lax.axis_size("fsdp")
    dp_count = lax.axis_size("dp")
    rows = out_weight.shape[0]
    half_rows = rows // 2
    core = lax.axis_index("dp") % 2
    gathered = lax.all_gather(out_weight, "fsdp", axis=0, tiled=True)
    taps = tap_mask(lengths[0], frames, count)
    live = taps[half_width][:, None]
    views = shifted(hidden_in, half_width)
    mixed = jnp.zeros((frames, chans), jnp.float32)
    for k in range(count):
        mixed = mixed + conv_kernel[k] * views[k].astype(jnp.float32) * taps[k][:, None]
    centred = mixed - jnp.mean(mixed, axis=-1, keepdims=True)
    inverse = lax.rsqrt(jnp.mean(centred * centred, axis=-1, keepdims=True) + 1e-05)
    normed = centred * inverse
    scaled = normed * norm_gain
    squash = jax.nn.sigmoid(scaled)
    activation = (scaled * squash * live).astype(jnp.bfloat16)
    split_act = activation.reshape(frames, fsdp_count, 2, half_rows)
    keep_act = lax.dynamic_index_in_dim(split_act, core, 2, keepdims=False).reshape(frames, -1)
    send_act = lax.dynamic_index_in_dim(split_act, 1 - core, 2, keepdims=False).reshape(frames, -1)
    contract = (((0,), (0,)), ((), ()))
    keep_terms = lax.dot_general(keep_act, grad_out, contract, preferred_element_type=jnp.float32)
    send_terms = lax.dot_general(send_act, grad_out, contract, preferred_element_type=jnp.float32)
    chip_terms = keep_terms + sibling(send_terms)
    gathered, chip_terms, activation = lax.optimization_barrier((gathered, chip_terms, activation))
    shard_sum = lax.psum_scatter(chip_terms, "fsdp", scatter_dimension=0, tiled=True)
    full_weight = gathered
    output = jnp.dot(activation, full_weight, preferred_element_type=jnp.float32)
    grad_act = lax.dot_general(
        grad_out, full_weight, (((1,), (1,)), ((), ())), preferred_element_type=jnp.float32
    )
    grad_scaled = grad_act * live * squash * (1.0 + scaled * (1.0 - squash))
    gain_grad = jnp.sum(grad_scaled * normed, axis=0)
    grad_normed = grad_scaled * norm_gain
    grad_mixed = inverse * (
        grad_normed
        - jnp.mean(grad_normed, axis=-1, keepdims=True)
        - normed * jnp.mean(grad_normed * normed, axis=-1, keepdims=True)
    )
    kernel_rows = []
    for k in range(count):
        weighted = grad_mixed * taps[k][:, None]
        kernel_rows.append(jnp.sum(weighted * views[k].astype(jnp.float32), axis=0))
    back_views = shifted(grad_mixed, half_width)
    grad_hidden = jnp.zeros((frames, chans), jnp.float32)
    for k in range(count):
        grad_hidden = grad_hidden + conv_kernel[k] * (
            back_views[count - 1 - k] * taps[count - 1 - k][:, None]
        )
    small = jnp.concatenate([jnp.stack(kernel_rows), gain_grad[None]], axis=0)
    small = butterfly(small, "fsdp", (1, 2, 4, 8))
    small = butterfly(small, "dp", (1, 2, 4, 8))
    shard_sum, small, output, grad_hidden = lax.optimization_barrier(
        (shard_sum, small, output, grad_hidden)
    )
    half_sum = butterfly(shard_sum, "dp", (2, 4, 8))
    other_sum = sibling(half_sum)
    weight_sum = jnp.where(
        core == 0,
        jnp.concatenate([half_sum, other_sum], axis=0),
        jnp.concatenate([other_sum, half_sum], axis=0),
    )
    factor = 1.0 / math.sqrt(frames * dp_count * fsdp_count)
    return (
        output,
        grad_hidden,
        weight_sum * factor,
        small[:count] * factor,
        small[count] * factor,
    )


def solution(mesh):
    placed = (
        P(("dp", "fsdp"), None),
        P(("dp", "fsdp"), None),
        P(("dp", "fsdp"), None),
        P(),
        P(),
        P("fsdp", None),
    )
    return jax.shard_map(
        shards,
        mesh=mesh,
        in_specs=placed,
        out_specs=(P(("dp", "fsdp"), None), P(("dp", "fsdp"), None), P("fsdp", None), P(), P()),
        check_vma=False,
    )
```

```python
import math

import jax
import jax.numpy as jnp
from jax import lax
from jax.sharding import PartitionSpec as P


def tap_mask(lengths, frames, count):
    utt_ends = jnp.cumsum(lengths)
    position = jnp.arange(frames, dtype=jnp.int32)
    segment_id = jnp.sum((position[:, None] >= utt_ends[None, :]).astype(jnp.int32), axis=1)
    inside = position < utt_ends[-1]
    half_width = count // 2
    segment_pad = jnp.pad(segment_id, half_width, constant_values=-1)
    inside_pad = jnp.pad(inside, half_width, constant_values=False)
    rows_out = []
    for k in range(count):
        same = (segment_pad[k : k + frames] == segment_id) & inside_pad[k : k + frames] & inside
        rows_out.append(same.astype(jnp.float32))
    return jnp.stack(rows_out)


def shifted(x, half_width):
    frames = x.shape[0]
    padded = jnp.pad(x, ((half_width, half_width), (0, 0)))
    return [padded[k : k + frames] for k in range(2 * half_width + 1)]


def butterfly(x, axis, steps):
    size = lax.axis_size(axis)
    for step in steps:
        pairs = [(i, i ^ step) for i in range(size)]
        x = x + lax.ppermute(x, axis, pairs)
    return x


def sibling(x):
    size = lax.axis_size("dp")
    return lax.ppermute(x, "dp", [(i, i ^ 1) for i in range(size)])


def doubling_step(held, axis, mask):
    size = lax.axis_size(axis)
    upper = (lax.axis_index(axis) & mask) != 0
    received = lax.ppermute(held, axis, [(i, i ^ mask) for i in range(size)])
    return jnp.where(
        upper,
        jnp.concatenate([received, held], axis=0),
        jnp.concatenate([held, received], axis=0),
    )


def doubling_order(held, masks):
    count = len(masks)
    bits = [int(math.log2(mask)) for mask in reversed(masks)]
    rest = held.shape[1:]
    held = held.reshape((2,) * count + rest)
    order = sorted(range(count), key=lambda axis_at: -bits[axis_at])
    held = jnp.transpose(held, order + [count + d for d in range(len(rest))])
    return held.reshape((-1,) + rest[1:])


def shards(hidden_in, grad_out, lengths, conv_kernel, norm_gain, out_weight):
    frames, chans = hidden_in.shape
    width = grad_out.shape[1]
    count = conv_kernel.shape[0]
    half_width = count // 2
    fsdp_count = lax.axis_size("fsdp")
    dp_count = lax.axis_size("dp")
    rows = out_weight.shape[0]
    half_rows = rows // 2
    core = lax.axis_index("dp") % 2
    masks = (2, 8, 1, 4)
    own_half = lax.dynamic_slice_in_dim(out_weight, core * half_rows, half_rows, 0)
    held = doubling_step(own_half[None], "fsdp", masks[0])
    taps = tap_mask(lengths[0], frames, count)
    held, taps = lax.optimization_barrier((held, taps))
    held = doubling_step(held, "fsdp", masks[1])
    live = taps[half_width][:, None]
    views = shifted(hidden_in, half_width)
    mixed = jnp.zeros((frames, chans), jnp.float32)
    for k in range(count):
        mixed = mixed + conv_kernel[k] * views[k].astype(jnp.float32) * taps[k][:, None]
    held, mixed = lax.optimization_barrier((held, mixed))
    held = doubling_step(held, "fsdp", masks[2])
    centred = mixed - jnp.mean(mixed, axis=-1, keepdims=True)
    inverse = lax.rsqrt(jnp.mean(centred * centred, axis=-1, keepdims=True) + 1e-05)
    normed = centred * inverse
    scaled = normed * norm_gain
    squash = jax.nn.sigmoid(scaled)
    activation = (scaled * squash * live).astype(jnp.bfloat16)
    split_act = activation.reshape(frames, fsdp_count, 2, half_rows)
    keep_act = lax.dynamic_index_in_dim(split_act, core, 2, keepdims=False).reshape(frames, -1)
    send_act = lax.dynamic_index_in_dim(split_act, 1 - core, 2, keepdims=False).reshape(frames, -1)
    contract = (((0,), (0,)), ((), ()))
    keep_terms = lax.dot_general(keep_act, grad_out, contract, preferred_element_type=jnp.float32)
    send_terms = lax.dot_general(send_act, grad_out, contract, preferred_element_type=jnp.float32)
    held, keep_terms, send_terms, activation = lax.optimization_barrier(
        (held, keep_terms, send_terms, activation)
    )
    held = doubling_step(held, "fsdp", masks[3])
    chip_terms = keep_terms + sibling(send_terms)
    shard_sum = lax.psum_scatter(chip_terms, "fsdp", scatter_dimension=0, tiled=True)
    held, chip_terms = lax.optimization_barrier((held, chip_terms))
    gathered = doubling_order(held, masks)
    other = sibling(gathered)
    first = jnp.where(core == 0, gathered, other).reshape(fsdp_count, 1, half_rows, width)
    second = jnp.where(core == 0, other, gathered).reshape(fsdp_count, 1, half_rows, width)
    full_weight = jnp.concatenate([first, second], axis=1).reshape(chans, width)
    output = jnp.dot(activation, full_weight, preferred_element_type=jnp.float32)
    grad_act = lax.dot_general(
        grad_out, full_weight, (((1,), (1,)), ((), ())), preferred_element_type=jnp.float32
    )
    grad_scaled = grad_act * live * squash * (1.0 + scaled * (1.0 - squash))
    gain_grad = jnp.sum(grad_scaled * normed, axis=0)
    grad_normed = grad_scaled * norm_gain
    grad_mixed = inverse * (
        grad_normed
        - jnp.mean(grad_normed, axis=-1, keepdims=True)
        - normed * jnp.mean(grad_normed * normed, axis=-1, keepdims=True)
    )
    kernel_rows = []
    for k in range(count):
        weighted = grad_mixed * taps[k][:, None]
        kernel_rows.append(jnp.sum(weighted * views[k].astype(jnp.float32), axis=0))
    back_views = shifted(grad_mixed, half_width)
    grad_hidden = jnp.zeros((frames, chans), jnp.float32)
    for k in range(count):
        grad_hidden = grad_hidden + conv_kernel[k] * (
            back_views[count - 1 - k] * taps[count - 1 - k][:, None]
        )
    small = jnp.concatenate([jnp.stack(kernel_rows), gain_grad[None]], axis=0)
    small = butterfly(small, "fsdp", (1, 2, 4, 8))
    small = butterfly(small, "dp", (1, 2, 4, 8))
    shard_sum, small, output, grad_hidden = lax.optimization_barrier(
        (shard_sum, small, output, grad_hidden)
    )
    half_sum = butterfly(shard_sum, "dp", (2, 4, 8))
    other_sum = sibling(half_sum)
    weight_sum = jnp.where(
        core == 0,
        jnp.concatenate([half_sum, other_sum], axis=0),
        jnp.concatenate([other_sum, half_sum], axis=0),
    )
    factor = 1.0 / math.sqrt(frames * dp_count * fsdp_count)
    return (
        output,
        grad_hidden,
        weight_sum * factor,
        small[:count] * factor,
        small[count] * factor,
    )


def solution(mesh):
    placed = (
        P(("dp", "fsdp"), None),
        P(("dp", "fsdp"), None),
        P(("dp", "fsdp"), None),
        P(),
        P(),
        P("fsdp", None),
    )
    return jax.shard_map(
        shards,
        mesh=mesh,
        in_specs=placed,
        out_specs=(P(("dp", "fsdp"), None), P(("dp", "fsdp"), None), P("fsdp", None), P(), P()),
        check_vma=False,
    )
```

```python
import math

import jax
import jax.numpy as jnp
from jax import lax
from jax.sharding import PartitionSpec as P


def tap_mask(lengths, frames, count):
    utt_ends = jnp.cumsum(lengths)
    position = jnp.arange(frames, dtype=jnp.int32)
    segment_id = jnp.sum((position[:, None] >= utt_ends[None, :]).astype(jnp.int32), axis=1)
    inside = position < utt_ends[-1]
    half_width = count // 2
    segment_pad = jnp.pad(segment_id, half_width, constant_values=-1)
    inside_pad = jnp.pad(inside, half_width, constant_values=False)
    rows_out = []
    for k in range(count):
        same = (segment_pad[k : k + frames] == segment_id) & inside_pad[k : k + frames] & inside
        rows_out.append(same.astype(jnp.float32))
    return jnp.stack(rows_out)


def shifted(x, half_width):
    frames = x.shape[0]
    padded = jnp.pad(x, ((half_width, half_width), (0, 0)))
    return [padded[k : k + frames] for k in range(2 * half_width + 1)]


def butterfly(x, axis, steps):
    size = lax.axis_size(axis)
    for step in steps:
        pairs = [(i, i ^ step) for i in range(size)]
        x = x + lax.ppermute(x, axis, pairs)
    return x


def sibling(x):
    size = lax.axis_size("dp")
    return lax.ppermute(x, "dp", [(i, i ^ 1) for i in range(size)])


def doubling_step(held, axis, mask):
    size = lax.axis_size(axis)
    upper = (lax.axis_index(axis) & mask) != 0
    received = lax.ppermute(held, axis, [(i, i ^ mask) for i in range(size)])
    return jnp.where(
        upper,
        jnp.concatenate([received, held], axis=0),
        jnp.concatenate([held, received], axis=0),
    )


def doubling_order(held, masks):
    count = len(masks)
    bits = [int(math.log2(mask)) for mask in reversed(masks)]
    rest = held.shape[1:]
    held = held.reshape((2,) * count + rest)
    order = sorted(range(count), key=lambda axis_at: -bits[axis_at])
    held = jnp.transpose(held, order + [count + d for d in range(len(rest))])
    return held.reshape((-1,) + rest[1:])


def shards(hidden_in, grad_out, lengths, conv_kernel, norm_gain, out_weight):
    frames, chans = hidden_in.shape
    width = grad_out.shape[1]
    count = conv_kernel.shape[0]
    half_width = count // 2
    fsdp_count = lax.axis_size("fsdp")
    dp_count = lax.axis_size("dp")
    rows = out_weight.shape[0]
    half_rows = rows // 2
    core = lax.axis_index("dp") % 2
    masks = (2, 8, 1, 4)
    own_half = lax.dynamic_slice_in_dim(out_weight, core * half_rows, half_rows, 0)
    held = doubling_step(own_half[None], "fsdp", masks[0])
    taps = tap_mask(lengths[0], frames, count)
    held, taps = lax.optimization_barrier((held, taps))
    held = doubling_step(held, "fsdp", masks[1])
    live = taps[half_width][:, None]
    views = shifted(hidden_in, half_width)
    mixed = jnp.zeros((frames, chans), jnp.float32)
    for k in range(count):
        mixed = mixed + conv_kernel[k] * views[k].astype(jnp.float32) * taps[k][:, None]
    held, mixed = lax.optimization_barrier((held, mixed))
    held = doubling_step(held, "fsdp", masks[2])
    centred = mixed - jnp.mean(mixed, axis=-1, keepdims=True)
    inverse = lax.rsqrt(jnp.mean(centred * centred, axis=-1, keepdims=True) + 1e-05)
    normed = centred * inverse
    scaled = normed * norm_gain
    squash = jax.nn.sigmoid(scaled)
    activation = (scaled * squash * live).astype(jnp.bfloat16)
    split_act = activation.reshape(frames, fsdp_count, 2, half_rows)
    keep_act = lax.dynamic_index_in_dim(split_act, core, 2, keepdims=False).reshape(frames, -1)
    send_act = lax.dynamic_index_in_dim(split_act, 1 - core, 2, keepdims=False).reshape(frames, -1)
    contract = (((0,), (0,)), ((), ()))
    keep_terms = lax.dot_general(keep_act, grad_out, contract, preferred_element_type=jnp.float32)
    send_terms = lax.dot_general(send_act, grad_out, contract, preferred_element_type=jnp.float32)
    chip_terms = keep_terms + sibling(send_terms)
    held, chip_terms, activation = lax.optimization_barrier((held, chip_terms, activation))
    shard_sum = lax.psum_scatter(chip_terms, "fsdp", scatter_dimension=0, tiled=True)
    held = doubling_step(held, "fsdp", masks[3])
    held, chip_terms = lax.optimization_barrier((held, chip_terms))
    gathered = doubling_order(held, masks)
    other = sibling(gathered)
    first = jnp.where(core == 0, gathered, other).reshape(fsdp_count, 1, half_rows, width)
    second = jnp.where(core == 0, other, gathered).reshape(fsdp_count, 1, half_rows, width)
    full_weight = jnp.concatenate([first, second], axis=1).reshape(chans, width)
    output = jnp.dot(activation, full_weight, preferred_element_type=jnp.float32)
    grad_act = lax.dot_general(
        grad_out, full_weight, (((1,), (1,)), ((), ())), preferred_element_type=jnp.float32
    )
    grad_scaled = grad_act * live * squash * (1.0 + scaled * (1.0 - squash))
    gain_grad = jnp.sum(grad_scaled * normed, axis=0)
    grad_normed = grad_scaled * norm_gain
    grad_mixed = inverse * (
        grad_normed
        - jnp.mean(grad_normed, axis=-1, keepdims=True)
        - normed * jnp.mean(grad_normed * normed, axis=-1, keepdims=True)
    )
    kernel_rows = []
    for k in range(count):
        weighted = grad_mixed * taps[k][:, None]
        kernel_rows.append(jnp.sum(weighted * views[k].astype(jnp.float32), axis=0))
    back_views = shifted(grad_mixed, half_width)
    grad_hidden = jnp.zeros((frames, chans), jnp.float32)
    for k in range(count):
        grad_hidden = grad_hidden + conv_kernel[k] * (
            back_views[count - 1 - k] * taps[count - 1 - k][:, None]
        )
    small = jnp.concatenate([jnp.stack(kernel_rows), gain_grad[None]], axis=0)
    small = butterfly(small, "fsdp", (1, 2, 4, 8))
    small, output, grad_hidden = lax.optimization_barrier((small, output, grad_hidden))
    small = butterfly(small, "dp", (1, 2, 4, 8))
    shard_sum, small, output, grad_hidden = lax.optimization_barrier(
        (shard_sum, small, output, grad_hidden)
    )
    half_sum = butterfly(shard_sum, "dp", (2, 4, 8))
    other_sum = sibling(half_sum)
    weight_sum = jnp.where(
        core == 0,
        jnp.concatenate([half_sum, other_sum], axis=0),
        jnp.concatenate([other_sum, half_sum], axis=0),
    )
    factor = 1.0 / math.sqrt(frames * dp_count * fsdp_count)
    return (
        output,
        grad_hidden,
        weight_sum * factor,
        small[:count] * factor,
        small[count] * factor,
    )


def solution(mesh):
    placed = (
        P(("dp", "fsdp"), None),
        P(("dp", "fsdp"), None),
        P(("dp", "fsdp"), None),
        P(),
        P(),
        P("fsdp", None),
    )
    return jax.shard_map(
        shards,
        mesh=mesh,
        in_specs=placed,
        out_specs=(P(("dp", "fsdp"), None), P(("dp", "fsdp"), None), P("fsdp", None), P(), P()),
        check_vma=False,
    )
```

```python
import math

import jax
import jax.numpy as jnp
from jax import lax
from jax.sharding import PartitionSpec as P


def tap_mask(lengths, frames, count):
    utt_ends = jnp.cumsum(lengths)
    position = jnp.arange(frames, dtype=jnp.int32)
    segment_id = jnp.sum((position[:, None] >= utt_ends[None, :]).astype(jnp.int32), axis=1)
    inside = position < utt_ends[-1]
    half_width = count // 2
    segment_pad = jnp.pad(segment_id, half_width, constant_values=-1)
    inside_pad = jnp.pad(inside, half_width, constant_values=False)
    rows_out = []
    for k in range(count):
        same = (segment_pad[k : k + frames] == segment_id) & inside_pad[k : k + frames] & inside
        rows_out.append(same.astype(jnp.float32))
    return jnp.stack(rows_out)


def shifted(x, half_width):
    frames = x.shape[0]
    padded = jnp.pad(x, ((half_width, half_width), (0, 0)))
    return [padded[k : k + frames] for k in range(2 * half_width + 1)]


def butterfly(x, axis, steps):
    size = lax.axis_size(axis)
    for step in steps:
        pairs = [(i, i ^ step) for i in range(size)]
        x = x + lax.ppermute(x, axis, pairs)
    return x


def sibling(x):
    size = lax.axis_size("dp")
    return lax.ppermute(x, "dp", [(i, i ^ 1) for i in range(size)])


def doubling_step(held, axis, mask):
    size = lax.axis_size(axis)
    upper = (lax.axis_index(axis) & mask) != 0
    received = lax.ppermute(held, axis, [(i, i ^ mask) for i in range(size)])
    return jnp.where(
        upper,
        jnp.concatenate([received, held], axis=0),
        jnp.concatenate([held, received], axis=0),
    )


def doubling_order(held, masks):
    count = len(masks)
    bits = [int(math.log2(mask)) for mask in reversed(masks)]
    rest = held.shape[1:]
    held = held.reshape((2,) * count + rest)
    order = sorted(range(count), key=lambda axis_at: -bits[axis_at])
    held = jnp.transpose(held, order + [count + d for d in range(len(rest))])
    return held.reshape((-1,) + rest[1:])


def shards(hidden_in, grad_out, lengths, conv_kernel, norm_gain, out_weight):
    frames, chans = hidden_in.shape
    width = grad_out.shape[1]
    count = conv_kernel.shape[0]
    half_width = count // 2
    fsdp_count = lax.axis_size("fsdp")
    dp_count = lax.axis_size("dp")
    rows = out_weight.shape[0]
    half_rows = rows // 2
    core = lax.axis_index("dp") % 2
    masks = (2, 8, 1, 4)
    own_half = lax.dynamic_slice_in_dim(out_weight, core * half_rows, half_rows, 0)
    held = doubling_step(own_half[None], "fsdp", masks[0])
    taps = tap_mask(lengths[0], frames, count)
    held, taps = lax.optimization_barrier((held, taps))
    held = doubling_step(held, "fsdp", masks[1])
    live = taps[half_width][:, None]
    views = shifted(hidden_in, half_width)
    mixed = jnp.zeros((frames, chans), jnp.float32)
    for k in range(count):
        mixed = mixed + conv_kernel[k] * views[k].astype(jnp.float32) * taps[k][:, None]
    held, mixed = lax.optimization_barrier((held, mixed))
    held = doubling_step(held, "fsdp", masks[2])
    centred = mixed - jnp.mean(mixed, axis=-1, keepdims=True)
    inverse = lax.rsqrt(jnp.mean(centred * centred, axis=-1, keepdims=True) + 1e-05)
    normed = centred * inverse
    scaled = normed * norm_gain
    squash = jax.nn.sigmoid(scaled)
    activation = (scaled * squash * live).astype(jnp.bfloat16)
    split_act = activation.reshape(frames, fsdp_count, 2, half_rows)
    keep_act = lax.dynamic_index_in_dim(split_act, core, 2, keepdims=False).reshape(frames, -1)
    send_act = lax.dynamic_index_in_dim(split_act, 1 - core, 2, keepdims=False).reshape(frames, -1)
    contract = (((0,), (0,)), ((), ()))
    keep_terms = lax.dot_general(keep_act, grad_out, contract, preferred_element_type=jnp.float32)
    send_terms = lax.dot_general(send_act, grad_out, contract, preferred_element_type=jnp.float32)
    held, keep_terms, send_terms, activation = lax.optimization_barrier(
        (held, keep_terms, send_terms, activation)
    )
    held = doubling_step(held, "fsdp", masks[3])
    chip_terms = keep_terms + sibling(send_terms)
    shard_sum = lax.psum_scatter(chip_terms, "fsdp", scatter_dimension=0, tiled=True)
    held, chip_terms = lax.optimization_barrier((held, chip_terms))
    gathered = doubling_order(held, masks)
    other = sibling(gathered)
    first = jnp.where(core == 0, gathered, other).reshape(fsdp_count, 1, half_rows, width)
    second = jnp.where(core == 0, other, gathered).reshape(fsdp_count, 1, half_rows, width)
    full_weight = jnp.concatenate([first, second], axis=1).reshape(chans, width)
    output = jnp.dot(activation, full_weight, preferred_element_type=jnp.float32)
    grad_act = lax.dot_general(
        grad_out, full_weight, (((1,), (1,)), ((), ())), preferred_element_type=jnp.float32
    )
    grad_scaled = grad_act * live * squash * (1.0 + scaled * (1.0 - squash))
    gain_grad = jnp.sum(grad_scaled * normed, axis=0)
    grad_normed = grad_scaled * norm_gain
    grad_mixed = inverse * (
        grad_normed
        - jnp.mean(grad_normed, axis=-1, keepdims=True)
        - normed * jnp.mean(grad_normed * normed, axis=-1, keepdims=True)
    )
    kernel_rows = []
    for k in range(count):
        weighted = grad_mixed * taps[k][:, None]
        kernel_rows.append(jnp.sum(weighted * views[k].astype(jnp.float32), axis=0))
    back_views = shifted(grad_mixed, half_width)
    grad_hidden = jnp.zeros((frames, chans), jnp.float32)
    for k in range(count):
        grad_hidden = grad_hidden + conv_kernel[k] * (
            back_views[count - 1 - k] * taps[count - 1 - k][:, None]
        )
    small = jnp.concatenate([jnp.stack(kernel_rows), gain_grad[None]], axis=0)
    small = butterfly(small, "fsdp", (1, 2, 4, 8))
    small = butterfly(small, "dp", (1,))
    shard_sum, small, output, grad_hidden = lax.optimization_barrier(
        (shard_sum, small, output, grad_hidden)
    )
    joined = butterfly(jnp.concatenate([shard_sum, small], axis=0), "dp", (2, 4, 8))
    half_sum = joined[: shard_sum.shape[0]]
    small = joined[shard_sum.shape[0] :]
    other_sum = sibling(half_sum)
    weight_sum = jnp.where(
        core == 0,
        jnp.concatenate([half_sum, other_sum], axis=0),
        jnp.concatenate([other_sum, half_sum], axis=0),
    )
    factor = 1.0 / math.sqrt(frames * dp_count * fsdp_count)
    return (
        output,
        grad_hidden,
        weight_sum * factor,
        small[:count] * factor,
        small[count] * factor,
    )


def solution(mesh):
    placed = (
        P(("dp", "fsdp"), None),
        P(("dp", "fsdp"), None),
        P(("dp", "fsdp"), None),
        P(),
        P(),
        P("fsdp", None),
    )
    return jax.shard_map(
        shards,
        mesh=mesh,
        in_specs=placed,
        out_specs=(P(("dp", "fsdp"), None), P(("dp", "fsdp"), None), P("fsdp", None), P(), P()),
        check_vma=False,
    )
```

```python
import math

import jax
import jax.numpy as jnp
from jax import lax
from jax.sharding import PartitionSpec as P


def tap_mask(lengths, frames, count):
    utt_ends = jnp.cumsum(lengths)
    position = jnp.arange(frames, dtype=jnp.int32)
    segment_id = jnp.sum((position[:, None] >= utt_ends[None, :]).astype(jnp.int32), axis=1)
    inside = position < utt_ends[-1]
    half_width = count // 2
    segment_pad = jnp.pad(segment_id, half_width, constant_values=-1)
    inside_pad = jnp.pad(inside, half_width, constant_values=False)
    rows_out = []
    for k in range(count):
        same = (segment_pad[k : k + frames] == segment_id) & inside_pad[k : k + frames] & inside
        rows_out.append(same.astype(jnp.float32))
    return jnp.stack(rows_out)


def shifted(x, half_width):
    frames = x.shape[0]
    padded = jnp.pad(x, ((half_width, half_width), (0, 0)))
    return [padded[k : k + frames] for k in range(2 * half_width + 1)]


def butterfly(x, axis, steps):
    size = lax.axis_size(axis)
    for step in steps:
        pairs = [(i, i ^ step) for i in range(size)]
        x = x + lax.ppermute(x, axis, pairs)
    return x


def sibling(x):
    size = lax.axis_size("dp")
    return lax.ppermute(x, "dp", [(i, i ^ 1) for i in range(size)])


def doubling_step(held, axis, mask):
    size = lax.axis_size(axis)
    upper = (lax.axis_index(axis) & mask) != 0
    received = lax.ppermute(held, axis, [(i, i ^ mask) for i in range(size)])
    return jnp.where(
        upper,
        jnp.concatenate([received, held], axis=0),
        jnp.concatenate([held, received], axis=0),
    )


def doubling_order(held, masks):
    count = len(masks)
    bits = [int(math.log2(mask)) for mask in reversed(masks)]
    rest = held.shape[1:]
    held = held.reshape((2,) * count + rest)
    order = sorted(range(count), key=lambda axis_at: -bits[axis_at])
    held = jnp.transpose(held, order + [count + d for d in range(len(rest))])
    return held.reshape((-1,) + rest[1:])


def shards(hidden_in, grad_out, lengths, conv_kernel, norm_gain, out_weight):
    frames, chans = hidden_in.shape
    width = grad_out.shape[1]
    count = conv_kernel.shape[0]
    half_width = count // 2
    fsdp_count = lax.axis_size("fsdp")
    dp_count = lax.axis_size("dp")
    rows = out_weight.shape[0]
    half_rows = rows // 2
    core = lax.axis_index("dp") % 2
    masks = (2, 8, 1, 4)
    own_half = lax.dynamic_slice_in_dim(out_weight, core * half_rows, half_rows, 0)
    held = doubling_step(own_half[None], "fsdp", masks[0])
    taps = tap_mask(lengths[0], frames, count)
    held, taps = lax.optimization_barrier((held, taps))
    held = doubling_step(held, "fsdp", masks[1])
    live = taps[half_width][:, None]
    views = shifted(hidden_in, half_width)
    mixed = jnp.zeros((frames, chans), jnp.float32)
    for k in range(count):
        mixed = mixed + conv_kernel[k] * views[k].astype(jnp.float32) * taps[k][:, None]
    held, mixed = lax.optimization_barrier((held, mixed))
    centred = mixed - jnp.mean(mixed, axis=-1, keepdims=True)
    inverse = lax.rsqrt(jnp.mean(centred * centred, axis=-1, keepdims=True) + 1e-05)
    normed = centred * inverse
    scaled = normed * norm_gain
    squash = jax.nn.sigmoid(scaled)
    activation = (scaled * squash * live).astype(jnp.bfloat16)
    split_act = activation.reshape(frames, fsdp_count, 2, half_rows)
    keep_act = lax.dynamic_index_in_dim(split_act, core, 2, keepdims=False).reshape(frames, -1)
    send_act = lax.dynamic_index_in_dim(split_act, 1 - core, 2, keepdims=False).reshape(frames, -1)
    contract = (((0,), (0,)), ((), ()))
    keep_terms = lax.dot_general(keep_act, grad_out, contract, preferred_element_type=jnp.float32)
    send_terms = lax.dot_general(send_act, grad_out, contract, preferred_element_type=jnp.float32)
    chip_terms = keep_terms + sibling(send_terms)
    held, chip_terms, activation = lax.optimization_barrier((held, chip_terms, activation))
    shard_sum = lax.psum_scatter(chip_terms, "fsdp", scatter_dimension=0, tiled=True)
    held = doubling_step(held, "fsdp", masks[2])
    held = doubling_step(held, "fsdp", masks[3])
    held, chip_terms = lax.optimization_barrier((held, chip_terms))
    gathered = doubling_order(held, masks)
    other = sibling(gathered)
    first = jnp.where(core == 0, gathered, other).reshape(fsdp_count, 1, half_rows, width)
    second = jnp.where(core == 0, other, gathered).reshape(fsdp_count, 1, half_rows, width)
    full_weight = jnp.concatenate([first, second], axis=1).reshape(chans, width)
    output = jnp.dot(activation, full_weight, preferred_element_type=jnp.float32)
    grad_act = lax.dot_general(
        grad_out, full_weight, (((1,), (1,)), ((), ())), preferred_element_type=jnp.float32
    )
    grad_scaled = grad_act * live * squash * (1.0 + scaled * (1.0 - squash))
    gain_grad = jnp.sum(grad_scaled * normed, axis=0)
    grad_normed = grad_scaled * norm_gain
    grad_mixed = inverse * (
        grad_normed
        - jnp.mean(grad_normed, axis=-1, keepdims=True)
        - normed * jnp.mean(grad_normed * normed, axis=-1, keepdims=True)
    )
    kernel_rows = []
    for k in range(count):
        weighted = grad_mixed * taps[k][:, None]
        kernel_rows.append(jnp.sum(weighted * views[k].astype(jnp.float32), axis=0))
    back_views = shifted(grad_mixed, half_width)
    grad_hidden = jnp.zeros((frames, chans), jnp.float32)
    for k in range(count):
        grad_hidden = grad_hidden + conv_kernel[k] * (
            back_views[count - 1 - k] * taps[count - 1 - k][:, None]
        )
    small = jnp.concatenate([jnp.stack(kernel_rows), gain_grad[None]], axis=0)
    small = butterfly(small, "fsdp", (1, 2, 4, 8))
    small = butterfly(small, "dp", (1,))
    shard_sum, small, output, grad_hidden = lax.optimization_barrier(
        (shard_sum, small, output, grad_hidden)
    )
    joined = butterfly(jnp.concatenate([shard_sum, small], axis=0), "dp", (2, 4, 8))
    half_sum = joined[: shard_sum.shape[0]]
    small = joined[shard_sum.shape[0] :]
    other_sum = sibling(half_sum)
    weight_sum = jnp.where(
        core == 0,
        jnp.concatenate([half_sum, other_sum], axis=0),
        jnp.concatenate([other_sum, half_sum], axis=0),
    )
    factor = 1.0 / math.sqrt(frames * dp_count * fsdp_count)
    return (
        output,
        grad_hidden,
        weight_sum * factor,
        small[:count] * factor,
        small[count] * factor,
    )


def solution(mesh):
    placed = (
        P(("dp", "fsdp"), None),
        P(("dp", "fsdp"), None),
        P(("dp", "fsdp"), None),
        P(),
        P(),
        P("fsdp", None),
    )
    return jax.shard_map(
        shards,
        mesh=mesh,
        in_specs=placed,
        out_specs=(P(("dp", "fsdp"), None), P(("dp", "fsdp"), None), P("fsdp", None), P(), P()),
        check_vma=False,
    )
```

```python
import math

import jax
import jax.numpy as jnp
from jax import lax
from jax.sharding import PartitionSpec as P


def tap_mask(lengths, frames, count):
    utt_ends = jnp.cumsum(lengths)
    position = jnp.arange(frames, dtype=jnp.int32)
    segment_id = jnp.sum((position[:, None] >= utt_ends[None, :]).astype(jnp.int32), axis=1)
    inside = position < utt_ends[-1]
    half_width = count // 2
    segment_pad = jnp.pad(segment_id, half_width, constant_values=-1)
    inside_pad = jnp.pad(inside, half_width, constant_values=False)
    rows_out = []
    for k in range(count):
        same = (segment_pad[k : k + frames] == segment_id) & inside_pad[k : k + frames] & inside
        rows_out.append(same.astype(jnp.float32))
    return jnp.stack(rows_out)


def shifted(x, half_width):
    frames = x.shape[0]
    padded = jnp.pad(x, ((half_width, half_width), (0, 0)))
    return [padded[k : k + frames] for k in range(2 * half_width + 1)]


def butterfly(x, axis, steps):
    size = lax.axis_size(axis)
    for step in steps:
        pairs = [(i, i ^ step) for i in range(size)]
        x = x + lax.ppermute(x, axis, pairs)
    return x


def sibling(x):
    size = lax.axis_size("dp")
    return lax.ppermute(x, "dp", [(i, i ^ 1) for i in range(size)])


def doubling_step(held, axis, mask):
    size = lax.axis_size(axis)
    upper = (lax.axis_index(axis) & mask) != 0
    received = lax.ppermute(held, axis, [(i, i ^ mask) for i in range(size)])
    return jnp.where(
        upper,
        jnp.concatenate([received, held], axis=0),
        jnp.concatenate([held, received], axis=0),
    )


def doubling_order(held, masks):
    count = len(masks)
    bits = [int(math.log2(mask)) for mask in reversed(masks)]
    rest = held.shape[1:]
    held = held.reshape((2,) * count + rest)
    order = sorted(range(count), key=lambda axis_at: -bits[axis_at])
    held = jnp.transpose(held, order + [count + d for d in range(len(rest))])
    return held.reshape((-1,) + rest[1:])


def shards(hidden_in, grad_out, lengths, conv_kernel, norm_gain, out_weight):
    frames, chans = hidden_in.shape
    width = grad_out.shape[1]
    count = conv_kernel.shape[0]
    half_width = count // 2
    fsdp_count = lax.axis_size("fsdp")
    dp_count = lax.axis_size("dp")
    rows = out_weight.shape[0]
    half_rows = rows // 2
    core = lax.axis_index("dp") % 2
    masks = (2, 8, 1, 4)
    own_half = lax.dynamic_slice_in_dim(out_weight, core * half_rows, half_rows, 0)
    held = doubling_step(own_half[None], "fsdp", masks[0])
    taps = tap_mask(lengths[0], frames, count)
    sibling_cot = sibling(grad_out)
    held, taps, sibling_cot = lax.optimization_barrier((held, taps, sibling_cot))
    held = doubling_step(held, "fsdp", masks[1])
    live = taps[half_width][:, None]
    views = shifted(hidden_in, half_width)
    mixed = jnp.zeros((frames, chans), jnp.float32)
    for k in range(count):
        mixed = mixed + conv_kernel[k] * views[k].astype(jnp.float32) * taps[k][:, None]
    held, mixed = lax.optimization_barrier((held, mixed))
    held = doubling_step(held, "fsdp", masks[2])
    centred = mixed - jnp.mean(mixed, axis=-1, keepdims=True)
    inverse = lax.rsqrt(jnp.mean(centred * centred, axis=-1, keepdims=True) + 1e-05)
    normed = centred * inverse
    scaled = normed * norm_gain
    squash = jax.nn.sigmoid(scaled)
    activation = (scaled * squash * live).astype(jnp.bfloat16)
    split_act = activation.reshape(frames, fsdp_count, 2, half_rows)
    keep_act = lax.dynamic_index_in_dim(split_act, core, 2, keepdims=False).reshape(frames, -1)
    send_act = lax.dynamic_index_in_dim(split_act, 1 - core, 2, keepdims=False).reshape(frames, -1)
    held, keep_act, send_act, activation = lax.optimization_barrier(
        (held, keep_act, send_act, activation)
    )
    held = doubling_step(held, "fsdp", masks[3])
    chip_act = jnp.concatenate([keep_act, sibling(send_act)], axis=0)
    chip_cot = jnp.concatenate([grad_out, sibling_cot], axis=0)
    chip_terms = lax.dot_general(
        chip_act, chip_cot, (((0,), (0,)), ((), ())), preferred_element_type=jnp.float32
    )
    shard_sum = lax.psum_scatter(chip_terms, "fsdp", scatter_dimension=0, tiled=True)
    held, chip_terms = lax.optimization_barrier((held, chip_terms))
    gathered = doubling_order(held, masks)
    other = sibling(gathered)
    first = jnp.where(core == 0, gathered, other).reshape(fsdp_count, 1, half_rows, width)
    second = jnp.where(core == 0, other, gathered).reshape(fsdp_count, 1, half_rows, width)
    full_weight = jnp.concatenate([first, second], axis=1).reshape(chans, width)
    output = jnp.dot(activation, full_weight, preferred_element_type=jnp.float32)
    grad_act = lax.dot_general(
        grad_out, full_weight, (((1,), (1,)), ((), ())), preferred_element_type=jnp.float32
    )
    grad_scaled = grad_act * live * squash * (1.0 + scaled * (1.0 - squash))
    gain_grad = jnp.sum(grad_scaled * normed, axis=0)
    grad_normed = grad_scaled * norm_gain
    grad_mixed = inverse * (
        grad_normed
        - jnp.mean(grad_normed, axis=-1, keepdims=True)
        - normed * jnp.mean(grad_normed * normed, axis=-1, keepdims=True)
    )
    kernel_rows = []
    for k in range(count):
        weighted = grad_mixed * taps[k][:, None]
        kernel_rows.append(jnp.sum(weighted * views[k].astype(jnp.float32), axis=0))
    back_views = shifted(grad_mixed, half_width)
    grad_hidden = jnp.zeros((frames, chans), jnp.float32)
    for k in range(count):
        grad_hidden = grad_hidden + conv_kernel[k] * (
            back_views[count - 1 - k] * taps[count - 1 - k][:, None]
        )
    small = jnp.concatenate([jnp.stack(kernel_rows), gain_grad[None]], axis=0)
    small = butterfly(small, "fsdp", (1, 2, 4, 8))
    small = butterfly(small, "dp", (1,))
    shard_sum, small, output, grad_hidden = lax.optimization_barrier(
        (shard_sum, small, output, grad_hidden)
    )
    joined = butterfly(jnp.concatenate([shard_sum, small], axis=0), "dp", (2, 4, 8))
    half_sum = joined[: shard_sum.shape[0]]
    small = joined[shard_sum.shape[0] :]
    other_sum = sibling(half_sum)
    weight_sum = jnp.where(
        core == 0,
        jnp.concatenate([half_sum, other_sum], axis=0),
        jnp.concatenate([other_sum, half_sum], axis=0),
    )
    factor = 1.0 / math.sqrt(frames * dp_count * fsdp_count)
    return (
        output,
        grad_hidden,
        weight_sum * factor,
        small[:count] * factor,
        small[count] * factor,
    )


def solution(mesh):
    placed = (
        P(("dp", "fsdp"), None),
        P(("dp", "fsdp"), None),
        P(("dp", "fsdp"), None),
        P(),
        P(),
        P("fsdp", None),
    )
    return jax.shard_map(
        shards,
        mesh=mesh,
        in_specs=placed,
        out_specs=(P(("dp", "fsdp"), None), P(("dp", "fsdp"), None), P("fsdp", None), P(), P()),
        check_vma=False,
    )
```

```python
import math

import jax
import jax.numpy as jnp
from jax import lax
from jax.sharding import PartitionSpec as P


def tap_mask(lengths, frames, count):
    utt_ends = jnp.cumsum(lengths)
    position = jnp.arange(frames, dtype=jnp.int32)
    segment_id = jnp.sum((position[:, None] >= utt_ends[None, :]).astype(jnp.int32), axis=1)
    inside = position < utt_ends[-1]
    half_width = count // 2
    segment_pad = jnp.pad(segment_id, half_width, constant_values=-1)
    inside_pad = jnp.pad(inside, half_width, constant_values=False)
    rows_out = []
    for k in range(count):
        same = (segment_pad[k : k + frames] == segment_id) & inside_pad[k : k + frames] & inside
        rows_out.append(same.astype(jnp.float32))
    return jnp.stack(rows_out)


def shifted(x, half_width):
    frames = x.shape[0]
    padded = jnp.pad(x, ((half_width, half_width), (0, 0)))
    return [padded[k : k + frames] for k in range(2 * half_width + 1)]


def butterfly(x, axis, steps):
    size = lax.axis_size(axis)
    for step in steps:
        pairs = [(i, i ^ step) for i in range(size)]
        x = x + lax.ppermute(x, axis, pairs)
    return x


def sibling(x):
    size = lax.axis_size("dp")
    return lax.ppermute(x, "dp", [(i, i ^ 1) for i in range(size)])


def doubling_step(held, axis, mask):
    size = lax.axis_size(axis)
    upper = (lax.axis_index(axis) & mask) != 0
    received = lax.ppermute(held, axis, [(i, i ^ mask) for i in range(size)])
    return jnp.where(
        upper,
        jnp.concatenate([received, held], axis=0),
        jnp.concatenate([held, received], axis=0),
    )


def doubling_order(held, masks):
    count = len(masks)
    bits = [int(math.log2(mask)) for mask in reversed(masks)]
    rest = held.shape[1:]
    held = held.reshape((2,) * count + rest)
    order = sorted(range(count), key=lambda axis_at: -bits[axis_at])
    held = jnp.transpose(held, order + [count + d for d in range(len(rest))])
    return held.reshape((-1,) + rest[1:])


def shards(hidden_in, grad_out, lengths, conv_kernel, norm_gain, out_weight):
    frames, chans = hidden_in.shape
    width = grad_out.shape[1]
    count = conv_kernel.shape[0]
    half_width = count // 2
    fsdp_count = lax.axis_size("fsdp")
    dp_count = lax.axis_size("dp")
    rows = out_weight.shape[0]
    half_rows = rows // 2
    core = lax.axis_index("dp") % 2
    masks = (2, 8, 1, 4)
    own_half = lax.dynamic_slice_in_dim(out_weight, core * half_rows, half_rows, 0)
    held = doubling_step(own_half[None], "fsdp", masks[0])
    taps = tap_mask(lengths[0], frames, count)
    sibling_cot = sibling(grad_out)
    held, taps, sibling_cot = lax.optimization_barrier((held, taps, sibling_cot))
    held = doubling_step(held, "fsdp", masks[1])
    live = taps[half_width][:, None]
    views = shifted(hidden_in, half_width)
    mixed = jnp.zeros((frames, chans), jnp.float32)
    for k in range(count):
        mixed = mixed + conv_kernel[k] * views[k].astype(jnp.float32) * taps[k][:, None]
    held, mixed = lax.optimization_barrier((held, mixed))
    held = doubling_step(held, "fsdp", masks[2])
    centred = mixed - jnp.mean(mixed, axis=-1, keepdims=True)
    inverse = lax.rsqrt(jnp.mean(centred * centred, axis=-1, keepdims=True) + 1e-05)
    normed = centred * inverse
    scaled = normed * norm_gain
    squash = jax.nn.sigmoid(scaled)
    activation = (scaled * squash * live).astype(jnp.bfloat16)
    split_act = activation.reshape(frames, fsdp_count, 2, half_rows)
    keep_act = lax.dynamic_index_in_dim(split_act, core, 2, keepdims=False).reshape(frames, -1)
    send_act = lax.dynamic_index_in_dim(split_act, 1 - core, 2, keepdims=False).reshape(frames, -1)
    chip_act = jnp.concatenate([keep_act, sibling(send_act)], axis=0)
    chip_cot = jnp.concatenate([grad_out, sibling_cot], axis=0)
    chip_terms = lax.dot_general(
        chip_act, chip_cot, (((0,), (0,)), ((), ())), preferred_element_type=jnp.float32
    )
    held, chip_terms, activation = lax.optimization_barrier((held, chip_terms, activation))
    held = doubling_step(held, "fsdp", masks[3])
    shard_sum = lax.psum_scatter(chip_terms, "fsdp", scatter_dimension=0, tiled=True)
    held, chip_terms = lax.optimization_barrier((held, chip_terms))
    gathered = doubling_order(held, masks)
    other = sibling(gathered)
    first = jnp.where(core == 0, gathered, other).reshape(fsdp_count, 1, half_rows, width)
    second = jnp.where(core == 0, other, gathered).reshape(fsdp_count, 1, half_rows, width)
    full_weight = jnp.concatenate([first, second], axis=1).reshape(chans, width)
    output = jnp.dot(activation, full_weight, preferred_element_type=jnp.float32)
    grad_act = lax.dot_general(
        grad_out, full_weight, (((1,), (1,)), ((), ())), preferred_element_type=jnp.float32
    )
    grad_scaled = grad_act * live * squash * (1.0 + scaled * (1.0 - squash))
    gain_grad = jnp.sum(grad_scaled * normed, axis=0)
    grad_normed = grad_scaled * norm_gain
    grad_mixed = inverse * (
        grad_normed
        - jnp.mean(grad_normed, axis=-1, keepdims=True)
        - normed * jnp.mean(grad_normed * normed, axis=-1, keepdims=True)
    )
    kernel_rows = []
    for k in range(count):
        weighted = grad_mixed * taps[k][:, None]
        kernel_rows.append(jnp.sum(weighted * views[k].astype(jnp.float32), axis=0))
    back_views = shifted(grad_mixed, half_width)
    grad_hidden = jnp.zeros((frames, chans), jnp.float32)
    for k in range(count):
        grad_hidden = grad_hidden + conv_kernel[k] * (
            back_views[count - 1 - k] * taps[count - 1 - k][:, None]
        )
    small = jnp.concatenate([jnp.stack(kernel_rows), gain_grad[None]], axis=0)
    small = butterfly(small, "fsdp", (1, 2, 4, 8))
    small = butterfly(small, "dp", (1,))
    shard_sum, small, output, grad_hidden = lax.optimization_barrier(
        (shard_sum, small, output, grad_hidden)
    )
    joined = butterfly(jnp.concatenate([shard_sum, small], axis=0), "dp", (2, 4, 8))
    half_sum = joined[: shard_sum.shape[0]]
    small = joined[shard_sum.shape[0] :]
    other_sum = sibling(half_sum)
    weight_sum = jnp.where(
        core == 0,
        jnp.concatenate([half_sum, other_sum], axis=0),
        jnp.concatenate([other_sum, half_sum], axis=0),
    )
    factor = 1.0 / math.sqrt(frames * dp_count * fsdp_count)
    return (
        output,
        grad_hidden,
        weight_sum * factor,
        small[:count] * factor,
        small[count] * factor,
    )


def solution(mesh):
    placed = (
        P(("dp", "fsdp"), None),
        P(("dp", "fsdp"), None),
        P(("dp", "fsdp"), None),
        P(),
        P(),
        P("fsdp", None),
    )
    return jax.shard_map(
        shards,
        mesh=mesh,
        in_specs=placed,
        out_specs=(P(("dp", "fsdp"), None), P(("dp", "fsdp"), None), P("fsdp", None), P(), P()),
        check_vma=False,
    )
```

```python
import math

import jax
import jax.numpy as jnp
from jax import lax
from jax.sharding import PartitionSpec as P


def tap_mask(lengths, frames, count):
    utt_ends = jnp.cumsum(lengths)
    position = jnp.arange(frames, dtype=jnp.int32)
    segment_id = jnp.sum((position[:, None] >= utt_ends[None, :]).astype(jnp.int32), axis=1)
    inside = position < utt_ends[-1]
    half_width = count // 2
    segment_pad = jnp.pad(segment_id, half_width, constant_values=-1)
    inside_pad = jnp.pad(inside, half_width, constant_values=False)
    rows_out = []
    for k in range(count):
        same = (segment_pad[k : k + frames] == segment_id) & inside_pad[k : k + frames] & inside
        rows_out.append(same.astype(jnp.float32))
    return jnp.stack(rows_out)


def shifted(x, half_width):
    frames = x.shape[0]
    padded = jnp.pad(x, ((half_width, half_width), (0, 0)))
    return [padded[k : k + frames] for k in range(2 * half_width + 1)]


def butterfly(x, axis, steps):
    size = lax.axis_size(axis)
    for step in steps:
        pairs = [(i, i ^ step) for i in range(size)]
        x = x + lax.ppermute(x, axis, pairs)
    return x


def sibling(x):
    size = lax.axis_size("dp")
    return lax.ppermute(x, "dp", [(i, i ^ 1) for i in range(size)])


def doubling_step(held, axis, mask):
    size = lax.axis_size(axis)
    upper = (lax.axis_index(axis) & mask) != 0
    received = lax.ppermute(held, axis, [(i, i ^ mask) for i in range(size)])
    return jnp.where(
        upper,
        jnp.concatenate([received, held], axis=0),
        jnp.concatenate([held, received], axis=0),
    )


def doubling_order(held, masks):
    count = len(masks)
    bits = [int(math.log2(mask)) for mask in reversed(masks)]
    rest = held.shape[1:]
    held = held.reshape((2,) * count + rest)
    order = sorted(range(count), key=lambda axis_at: -bits[axis_at])
    held = jnp.transpose(held, order + [count + d for d in range(len(rest))])
    return held.reshape((-1,) + rest[1:])


def shards(hidden_in, grad_out, lengths, conv_kernel, norm_gain, out_weight):
    frames, chans = hidden_in.shape
    width = grad_out.shape[1]
    count = conv_kernel.shape[0]
    half_width = count // 2
    fsdp_count = lax.axis_size("fsdp")
    dp_count = lax.axis_size("dp")
    rows = out_weight.shape[0]
    half_rows = rows // 2
    core = lax.axis_index("dp") % 2
    masks = (2, 8, 1, 4)
    own_half = lax.dynamic_slice_in_dim(out_weight, core * half_rows, half_rows, 0)
    held = doubling_step(own_half[None], "fsdp", masks[0])
    taps = tap_mask(lengths[0], frames, count)
    sibling_cot = sibling(grad_out)
    held, taps, sibling_cot = lax.optimization_barrier((held, taps, sibling_cot))
    held = doubling_step(held, "fsdp", masks[1])
    live = taps[half_width][:, None]
    views = shifted(hidden_in, half_width)
    mixed = jnp.zeros((frames, chans), jnp.float32)
    for k in range(count):
        mixed = mixed + conv_kernel[k] * views[k].astype(jnp.float32) * taps[k][:, None]
    held, mixed = lax.optimization_barrier((held, mixed))
    held = doubling_step(held, "fsdp", masks[2])
    centred = mixed - jnp.mean(mixed, axis=-1, keepdims=True)
    inverse = lax.rsqrt(jnp.mean(centred * centred, axis=-1, keepdims=True) + 1e-05)
    normed = centred * inverse
    scaled = normed * norm_gain
    squash = jax.nn.sigmoid(scaled)
    activation = (scaled * squash * live).astype(jnp.bfloat16)
    split_act = activation.reshape(frames, fsdp_count, 2, half_rows)
    keep_act = lax.dynamic_index_in_dim(split_act, core, 2, keepdims=False).reshape(frames, -1)
    send_act = lax.dynamic_index_in_dim(split_act, 1 - core, 2, keepdims=False).reshape(frames, -1)
    held, keep_act, send_act, activation = lax.optimization_barrier(
        (held, keep_act, send_act, activation)
    )
    held = doubling_step(held, "fsdp", masks[3])
    chip_act = jnp.concatenate([keep_act, sibling(send_act)], axis=0)
    chip_cot = jnp.concatenate([grad_out, sibling_cot], axis=0)
    factor = 1.0 / math.sqrt(frames * dp_count * fsdp_count)
    chip_terms = factor * lax.dot_general(
        chip_act, chip_cot, (((0,), (0,)), ((), ())), preferred_element_type=jnp.float32
    )
    shard_sum = lax.psum_scatter(chip_terms, "fsdp", scatter_dimension=0, tiled=True)
    held, chip_terms = lax.optimization_barrier((held, chip_terms))
    gathered = doubling_order(held, masks)
    other = sibling(gathered)
    first = jnp.where(core == 0, gathered, other).reshape(fsdp_count, 1, half_rows, width)
    second = jnp.where(core == 0, other, gathered).reshape(fsdp_count, 1, half_rows, width)
    full_weight = jnp.concatenate([first, second], axis=1).reshape(chans, width)
    output = jnp.dot(activation, full_weight, preferred_element_type=jnp.float32)
    grad_act = lax.dot_general(
        grad_out, full_weight, (((1,), (1,)), ((), ())), preferred_element_type=jnp.float32
    )
    grad_scaled = grad_act * live * squash * (1.0 + scaled * (1.0 - squash))
    gain_grad = jnp.sum(grad_scaled * normed, axis=0)
    grad_normed = grad_scaled * norm_gain
    grad_mixed = inverse * (
        grad_normed
        - jnp.mean(grad_normed, axis=-1, keepdims=True)
        - normed * jnp.mean(grad_normed * normed, axis=-1, keepdims=True)
    )
    kernel_rows = []
    for k in range(count):
        weighted = grad_mixed * taps[k][:, None]
        kernel_rows.append(jnp.sum(weighted * views[k].astype(jnp.float32), axis=0))
    back_views = shifted(grad_mixed, half_width)
    grad_hidden = jnp.zeros((frames, chans), jnp.float32)
    for k in range(count):
        grad_hidden = grad_hidden + conv_kernel[k] * (
            back_views[count - 1 - k] * taps[count - 1 - k][:, None]
        )
    small = factor * jnp.concatenate([jnp.stack(kernel_rows), gain_grad[None]], axis=0)
    small = butterfly(small, "fsdp", (1, 2, 4, 8))
    small = butterfly(small, "dp", (1,))
    shard_sum, small, output, grad_hidden = lax.optimization_barrier(
        (shard_sum, small, output, grad_hidden)
    )
    joined = butterfly(jnp.concatenate([shard_sum, small], axis=0), "dp", (2, 4, 8))
    half_sum = joined[: shard_sum.shape[0]]
    small = joined[shard_sum.shape[0] :]
    other_sum = sibling(half_sum)
    weight_sum = jnp.where(
        core == 0,
        jnp.concatenate([half_sum, other_sum], axis=0),
        jnp.concatenate([other_sum, half_sum], axis=0),
    )
    return (output, grad_hidden, weight_sum, small[:count], small[count])


def solution(mesh):
    placed = (
        P(("dp", "fsdp"), None),
        P(("dp", "fsdp"), None),
        P(("dp", "fsdp"), None),
        P(),
        P(),
        P("fsdp", None),
    )
    return jax.shard_map(
        shards,
        mesh=mesh,
        in_specs=placed,
        out_specs=(P(("dp", "fsdp"), None), P(("dp", "fsdp"), None), P("fsdp", None), P(), P()),
        check_vma=False,
    )
```

```python
import math

import jax
import jax.numpy as jnp
from jax import lax
from jax.sharding import PartitionSpec as P


def tap_mask(lengths, frames, count):
    utt_ends = jnp.cumsum(lengths)
    position = jnp.arange(frames, dtype=jnp.int32)
    segment_id = jnp.sum((position[:, None] >= utt_ends[None, :]).astype(jnp.int32), axis=1)
    inside = position < utt_ends[-1]
    half_width = count // 2
    segment_pad = jnp.pad(segment_id, half_width, constant_values=-1)
    inside_pad = jnp.pad(inside, half_width, constant_values=False)
    rows_out = []
    for k in range(count):
        same = (segment_pad[k : k + frames] == segment_id) & inside_pad[k : k + frames] & inside
        rows_out.append(same.astype(jnp.float32))
    return jnp.stack(rows_out)


def shifted(x, half_width):
    frames = x.shape[0]
    padded = jnp.pad(x, ((half_width, half_width), (0, 0)))
    return [padded[k : k + frames] for k in range(2 * half_width + 1)]


def butterfly(x, axis, steps):
    size = lax.axis_size(axis)
    for step in steps:
        pairs = [(i, i ^ step) for i in range(size)]
        x = x + lax.ppermute(x, axis, pairs)
    return x


def sibling(x):
    size = lax.axis_size("dp")
    return lax.ppermute(x, "dp", [(i, i ^ 1) for i in range(size)])


def doubling_step(held, axis, mask):
    size = lax.axis_size(axis)
    upper = (lax.axis_index(axis) & mask) != 0
    received = lax.ppermute(held, axis, [(i, i ^ mask) for i in range(size)])
    return jnp.where(
        upper,
        jnp.concatenate([received, held], axis=0),
        jnp.concatenate([held, received], axis=0),
    )


def doubling_order(held, masks):
    count = len(masks)
    bits = [int(math.log2(mask)) for mask in reversed(masks)]
    rest = held.shape[1:]
    held = held.reshape((2,) * count + rest)
    order = sorted(range(count), key=lambda axis_at: -bits[axis_at])
    held = jnp.transpose(held, order + [count + d for d in range(len(rest))])
    return held.reshape((-1,) + rest[1:])


def shards(hidden_in, grad_out, lengths, conv_kernel, norm_gain, out_weight):
    frames, chans = hidden_in.shape
    width = grad_out.shape[1]
    count = conv_kernel.shape[0]
    half_width = count // 2
    fsdp_count = lax.axis_size("fsdp")
    dp_count = lax.axis_size("dp")
    rows = out_weight.shape[0]
    half_rows = rows // 2
    core = lax.axis_index("dp") % 2
    masks = (2, 1, 8, 4)
    own_half = lax.dynamic_slice_in_dim(out_weight, core * half_rows, half_rows, 0)
    held = doubling_step(own_half[None], "fsdp", masks[0])
    taps = tap_mask(lengths[0], frames, count)
    sibling_cot = sibling(grad_out)
    held, taps, sibling_cot = lax.optimization_barrier((held, taps, sibling_cot))
    held = doubling_step(held, "fsdp", masks[1])
    live = taps[half_width][:, None]
    views = shifted(hidden_in, half_width)
    mixed = jnp.zeros((frames, chans), jnp.float32)
    for k in range(count):
        mixed = mixed + conv_kernel[k] * views[k].astype(jnp.float32) * taps[k][:, None]
    held, mixed = lax.optimization_barrier((held, mixed))
    held = doubling_step(held, "fsdp", masks[2])
    centred = mixed - jnp.mean(mixed, axis=-1, keepdims=True)
    inverse = lax.rsqrt(jnp.mean(centred * centred, axis=-1, keepdims=True) + 1e-05)
    normed = centred * inverse
    scaled = normed * norm_gain
    squash = jax.nn.sigmoid(scaled)
    activation = (scaled * squash * live).astype(jnp.bfloat16)
    split_act = activation.reshape(frames, fsdp_count, 2, half_rows)
    keep_act = lax.dynamic_index_in_dim(split_act, core, 2, keepdims=False).reshape(frames, -1)
    send_act = lax.dynamic_index_in_dim(split_act, 1 - core, 2, keepdims=False).reshape(frames, -1)
    held, keep_act, send_act, activation = lax.optimization_barrier(
        (held, keep_act, send_act, activation)
    )
    held = doubling_step(held, "fsdp", masks[3])
    chip_act = jnp.concatenate([keep_act, sibling(send_act)], axis=0)
    chip_cot = jnp.concatenate([grad_out, sibling_cot], axis=0)
    chip_terms = lax.dot_general(
        chip_act, chip_cot, (((0,), (0,)), ((), ())), preferred_element_type=jnp.float32
    )
    shard_sum = lax.psum_scatter(chip_terms, "fsdp", scatter_dimension=0, tiled=True)
    held, chip_terms = lax.optimization_barrier((held, chip_terms))
    gathered = doubling_order(held, masks)
    other = sibling(gathered)
    first = jnp.where(core == 0, gathered, other).reshape(fsdp_count, 1, half_rows, width)
    second = jnp.where(core == 0, other, gathered).reshape(fsdp_count, 1, half_rows, width)
    full_weight = jnp.concatenate([first, second], axis=1).reshape(chans, width)
    output = jnp.dot(activation, full_weight, preferred_element_type=jnp.float32)
    grad_act = lax.dot_general(
        grad_out, full_weight, (((1,), (1,)), ((), ())), preferred_element_type=jnp.float32
    )
    grad_scaled = grad_act * live * squash * (1.0 + scaled * (1.0 - squash))
    gain_grad = jnp.sum(grad_scaled * normed, axis=0)
    grad_normed = grad_scaled * norm_gain
    grad_mixed = inverse * (
        grad_normed
        - jnp.mean(grad_normed, axis=-1, keepdims=True)
        - normed * jnp.mean(grad_normed * normed, axis=-1, keepdims=True)
    )
    kernel_rows = []
    for k in range(count):
        weighted = grad_mixed * taps[k][:, None]
        kernel_rows.append(jnp.sum(weighted * views[k].astype(jnp.float32), axis=0))
    back_views = shifted(grad_mixed, half_width)
    grad_hidden = jnp.zeros((frames, chans), jnp.float32)
    for k in range(count):
        grad_hidden = grad_hidden + conv_kernel[k] * (
            back_views[count - 1 - k] * taps[count - 1 - k][:, None]
        )
    small = jnp.concatenate([jnp.stack(kernel_rows), gain_grad[None]], axis=0)
    small = butterfly(small, "fsdp", (1, 2, 4, 8))
    small = butterfly(small, "dp", (1,))
    shard_sum, small, output, grad_hidden = lax.optimization_barrier(
        (shard_sum, small, output, grad_hidden)
    )
    joined = butterfly(jnp.concatenate([shard_sum, small], axis=0), "dp", (2, 4, 8))
    half_sum = joined[: shard_sum.shape[0]]
    small = joined[shard_sum.shape[0] :]
    other_sum = sibling(half_sum)
    weight_sum = jnp.where(
        core == 0,
        jnp.concatenate([half_sum, other_sum], axis=0),
        jnp.concatenate([other_sum, half_sum], axis=0),
    )
    factor = 1.0 / math.sqrt(frames * dp_count * fsdp_count)
    return (
        output,
        grad_hidden,
        weight_sum * factor,
        small[:count] * factor,
        small[count] * factor,
    )


def solution(mesh):
    placed = (
        P(("dp", "fsdp"), None),
        P(("dp", "fsdp"), None),
        P(("dp", "fsdp"), None),
        P(),
        P(),
        P("fsdp", None),
    )
    return jax.shard_map(
        shards,
        mesh=mesh,
        in_specs=placed,
        out_specs=(P(("dp", "fsdp"), None), P(("dp", "fsdp"), None), P("fsdp", None), P(), P()),
        check_vma=False,
    )
```
